512 devices in a mesh: row: 64 (over y, x, core), col: 8 (over z).
Axes of the slice: x: 4, y: 8, z: 8, core: 2. Of those that a mesh axis runs over, the one named last changes fastest.
Arguments:
- panel_cols: float32 [16384, 256], P('row'), may hold values from -60 to 60, as said below
- affinity: float32 [16384, 16384], P('row', 'col'), may hold values from -8 to 8, as said below
Outputs:
- updated: float32 [16384, 16384], P('row', 'col')
- band_block: float32 [256, 256], replicated
The draws below stay inside these ranges and needn't reach their ends.
Inputs may be any that keep to these rules, and one draw needn't show every extreme that they name: affinity holds a symmetric matrix in the stored column order of the steps. panel_cols has full column rank.
All inputs are finite; a program needn't handle non-finite values.
Results may differ from the reference program's by a relative error of at most 0.000071.
Values sent between devices are 32-bit elements; how exact they have to be, the bound alone decides.
No kernel may reach another device: no remote copies, remote signals or barrier semaphores. Data moves between devices by JAX's collectives and lax.ppermute only.
A program may use at most 64 MiB of HBM per device.

```python
import math
import jax
import jax.numpy as jnp
from jax import lax

K = 256
N = 16384
PIECE = 32
N_ROW = 64
N_COL = 8


def draw_affinity(key, part):
    first_key = jax.random.fold_in(key, 0)
    random_part = jax.random.normal(first_key, (N, N), jnp.float32)
    symmetric = (random_part + random_part.T) * math.sqrt(0.5)
    symmetric = jnp.clip(symmetric, -8.0, 8.0)
    shaped = symmetric.reshape(N, N_ROW, N_COL, PIECE)
    return jnp.transpose(shaped, (0, 2, 1, 3)).reshape(N, N)


def draw_panel_cols(key, part):
    first_key = jax.random.fold_in(key, 0)
    row_rise = 1.0 + 2.0 * jnp.arange(N, dtype=jnp.float32)[:, None] / (N - 1)
    random_part = jnp.clip(jax.random.normal(first_key, (N, K), jnp.float32), -4.0, 4.0)
    return random_part * row_rise


def setup_inputs(seed: int = 0) -> dict:
    seeds = jax.random.split(jax.random.key(seed), 3)
    panel_cols = draw_panel_cols(jax.random.fold_in(seeds[2], 71), 0)
    affinity = draw_affinity(jax.random.fold_in(seeds[2], 71), 0)
    return {"panel_cols": panel_cols, "affinity": affinity}


def stored_order(rows_array):
    width = rows_array.shape[1]
    shaped = rows_array.reshape(N_ROW, N_COL, PIECE, width)
    return jnp.transpose(shaped, (1, 0, 2, 3)).reshape(N, width)

def reference(panel_cols, affinity):
    high = lax.Precision.HIGHEST
    gram_sum = jnp.dot(panel_cols.T, panel_cols, precision=high)
    lower_factor = jnp.linalg.cholesky(gram_sum)
    ortho_basis = jax.scipy.linalg.solve_triangular(lower_factor, panel_cols.T, lower=True).T
    basis_stored = stored_order(ortho_basis)
    moment = jnp.dot(affinity, basis_stored, precision=high)
    band_block = jnp.dot(ortho_basis.T, moment, precision=high)
    corrected = moment - 0.5 * jnp.dot(ortho_basis, band_block, precision=high)
    corrected_stored = stored_order(corrected)
    updated = affinity - jnp.dot(ortho_basis, corrected_stored.T, precision=high)
    updated = updated - jnp.dot(corrected, basis_stored.T, precision=high)
    return (updated, band_block)
```

```python
import jax
import jax.numpy as jnp
from jax import lax
from jax.sharding import PartitionSpec as P


def _dot(a, b):
    return jnp.dot(a, b, precision=lax.Precision.HIGHEST)


def _exchange(x, axis):
    return lax.all_to_all(x, axis, 0, 0, tiled=False)


def shards(panel_cols, affinity):
    local_rows, k = panel_cols.shape
    n_row = lax.axis_size("row")
    n_col = lax.axis_size("col")
    piece = local_rows // n_col
    col_place = lax.axis_index("col")

    gram_part = _dot(panel_cols.T, panel_cols)
    gram_rows = _exchange(gram_part.reshape(n_row, k // n_row, k), "row").sum(0)
    gram_sum = _exchange(jnp.broadcast_to(gram_rows[None], (n_row,) + gram_rows.shape), "row").reshape(k, k)

    own_panel = lax.dynamic_slice_in_dim(panel_cols, col_place * piece, piece, 0)
    panel_stored = _exchange(jnp.broadcast_to(own_panel[None], (n_row, piece, k)), "row").reshape(n_row * piece, k)

    lower_factor = jnp.linalg.cholesky(gram_sum)
    eye = jnp.eye(k, dtype=panel_cols.dtype)
    inv_lower = jax.scipy.linalg.solve_triangular(lower_factor, eye, lower=True)
    basis_own = _dot(panel_cols, inv_lower.T)
    basis_stored = _dot(panel_stored, inv_lower.T)

    partial_sum = _dot(affinity, basis_stored)
    gathered = _exchange(jnp.broadcast_to(partial_sum[None], (n_col,) + partial_sum.shape), "col")
    moment_own = gathered.sum(0)
    band_part = _dot(basis_own.T, moment_own)

    own_moment = lax.dynamic_slice_in_dim(moment_own, col_place * piece, piece, 0)
    send = jnp.concatenate(
        [
            jnp.broadcast_to(own_moment.reshape(1, piece * k), (n_row, piece * k)),
            band_part.reshape(n_row, (k // n_row) * k),
        ],
        axis=1,
    )
    got = _exchange(send, "row")
    moment_stored = got[:, : piece * k].reshape(n_row * piece, k)
    band_rows = got[:, piece * k :].sum(0)
    band_block = _exchange(jnp.broadcast_to(band_rows[None], (n_row,) + band_rows.shape), "row").reshape(k, k)

    corrected_own = moment_own - 0.5 * _dot(basis_own, band_block)
    corrected_stored = moment_stored - 0.5 * _dot(basis_stored, band_block)
    updated = affinity - _dot(basis_own, corrected_stored.T)
    updated = updated - _dot(corrected_own, basis_stored.T)
    return (updated, band_block)


def solution(mesh):
    placed = (P("row", None), P("row", "col"))
    return jax.shard_map(
        shards, mesh=mesh, in_specs=placed, out_specs=(P("row", "col"), P()), check_vma=False
    )
```

```python
import jax
import jax.numpy as jnp
from jax import lax
from jax.sharding import PartitionSpec as P


def _dot(a, b):
    return jnp.dot(a, b, precision=lax.Precision.HIGHEST)


def _exchange(x, axis):
    return lax.all_to_all(x, axis, 0, 0, tiled=False)


def shards(panel_cols, affinity):
    local_rows, k = panel_cols.shape
    n_row = lax.axis_size("row")
    n_col = lax.axis_size("col")
    piece = local_rows // n_col
    col_place = lax.axis_index("col")

    gram_part = _dot(panel_cols.T, panel_cols)
    gram_rows = _exchange(gram_part.reshape(n_row, k // n_row, k), "row").sum(0)
    gram_sum = _exchange(jnp.broadcast_to(gram_rows[None], (n_row,) + gram_rows.shape), "row").reshape(k, k)

    own_panel = lax.dynamic_slice_in_dim(panel_cols, col_place * piece, piece, 0)
    panel_stored = _exchange(jnp.broadcast_to(own_panel[None], (n_row, piece, k)), "row").reshape(n_row * piece, k)

    lower_factor = jnp.linalg.cholesky(gram_sum)
    eye = jnp.eye(k, dtype=panel_cols.dtype)
    inv_lower = jax.scipy.linalg.solve_triangular(lower_factor, eye, lower=True)
    basis_own = _dot(panel_cols, inv_lower.T)
    basis_stored = _dot(panel_stored, inv_lower.T)

    partial_sum = _dot(affinity, basis_stored)
    own_moment = _exchange(partial_sum.reshape(n_col, piece, k), "col").sum(0)
    moment_own = _exchange(jnp.broadcast_to(own_moment[None], (n_col, piece, k)), "col").reshape(local_rows, k)
    band_part = _dot(basis_own.T, moment_own)

    send = jnp.concatenate(
        [
            jnp.broadcast_to(own_moment.reshape(1, piece * k), (n_row, piece * k)),
            band_part.reshape(n_row, (k // n_row) * k),
        ],
        axis=1,
    )
    got = _exchange(send, "row")
    moment_stored = got[:, : piece * k].reshape(n_row * piece, k)
    band_rows = got[:, piece * k :].sum(0)
    band_block = _exchange(jnp.broadcast_to(band_rows[None], (n_row,) + band_rows.shape), "row").reshape(k, k)

    corrected_own = moment_own - 0.5 * _dot(basis_own, band_block)
    corrected_stored = moment_stored - 0.5 * _dot(basis_stored, band_block)
    updated = affinity - _dot(basis_own, corrected_stored.T)
    updated = updated - _dot(corrected_own, basis_stored.T)
    return (updated, band_block)


def solution(mesh):
    placed = (P("row", None), P("row", "col"))
    return jax.shard_map(
        shards, mesh=mesh, in_specs=placed, out_specs=(P("row", "col"), P()), check_vma=False
    )
```

```python
import jax
import jax.numpy as jnp
from jax import lax
from jax.sharding import PartitionSpec as P


def _dot(a, b):
    return jnp.dot(a, b, precision=lax.Precision.HIGHEST)


def _exchange(x, axis):
    return lax.all_to_all(x, axis, 0, 0, tiled=False)


def _inverse_cholesky(gram):
    h = gram.shape[0] // 2
    eye = jnp.eye(h, dtype=gram.dtype)
    l11 = jnp.linalg.cholesky(gram[:h, :h])
    i11 = jax.scipy.linalg.solve_triangular(l11, eye, lower=True)
    l21 = _dot(gram[h:, :h], i11.T)
    l22 = jnp.linalg.cholesky(gram[h:, h:] - _dot(l21, l21.T))
    i22 = jax.scipy.linalg.solve_triangular(l22, eye, lower=True)
    i21 = -_dot(i22, _dot(l21, i11))
    top = jnp.concatenate([i11, jnp.zeros_like(i11)], axis=1)
    return jnp.concatenate([top, jnp.concatenate([i21, i22], axis=1)], axis=0)


def shards(panel_cols, affinity):
    local_rows, k = panel_cols.shape
    n_row = lax.axis_size("row")
    n_col = lax.axis_size("col")
    piece = local_rows // n_col
    col_place = lax.axis_index("col")

    gram_part = _dot(panel_cols.T, panel_cols)
    gram_rows = _exchange(gram_part.reshape(n_row, k // n_row, k), "row").sum(0)
    gram_sum = _exchange(jnp.broadcast_to(gram_rows[None], (n_row,) + gram_rows.shape), "row").reshape(k, k)

    own_panel = lax.dynamic_slice_in_dim(panel_cols, col_place * piece, piece, 0)
    panel_stored = _exchange(jnp.broadcast_to(own_panel[None], (n_row, piece, k)), "row").reshape(n_row * piece, k)

    inv_lower = _inverse_cholesky(gram_sum)
    basis_own = _dot(panel_cols, inv_lower.T)
    basis_stored = _dot(panel_stored, inv_lower.T)

    partial_sum = _dot(affinity, basis_stored)
    own_moment = _exchange(partial_sum.reshape(n_col, piece, k), "col").sum(0)
    moment_own = _exchange(jnp.broadcast_to(own_moment[None], (n_col, piece, k)), "col").reshape(local_rows, k)
    band_part = _dot(basis_own.T, moment_own)

    send = jnp.concatenate(
        [
            jnp.broadcast_to(own_moment.reshape(1, piece * k), (n_row, piece * k)),
            band_part.reshape(n_row, (k // n_row) * k),
        ],
        axis=1,
    )
    got = _exchange(send, "row")
    moment_stored = got[:, : piece * k].reshape(n_row * piece, k)
    band_rows = got[:, piece * k :].sum(0)
    band_block = _exchange(jnp.broadcast_to(band_rows[None], (n_row,) + band_rows.shape), "row").reshape(k, k)

    corrected_own = moment_own - 0.5 * _dot(basis_own, band_block)
    corrected_stored = moment_stored - 0.5 * _dot(basis_stored, band_block)
    updated = affinity - _dot(basis_own, corrected_stored.T)
    updated = updated - _dot(corrected_own, basis_stored.T)
    return (updated, band_block)


def solution(mesh):
    placed = (P("row", None), P("row", "col"))
    return jax.shard_map(
        shards, mesh=mesh, in_specs=placed, out_specs=(P("row", "col"), P()), check_vma=False
    )
```

```python
import jax
import jax.numpy as jnp
from jax import lax
from jax.experimental import pallas as pl
from jax.experimental.pallas import tpu as pltpu
from jax.sharding import PartitionSpec as P


def _dot(a, b):
    return jnp.dot(a, b, precision=lax.Precision.HIGHEST)


def _exchange(x, axis):
    return lax.all_to_all(x, axis, 0, 0, tiled=False)


def _inverse_cholesky_kernel(g_ref, w_ref, a_ref):
    n = g_ref.shape[0]
    h = n // 2
    rows = lax.broadcasted_iota(jnp.int32, (n, n), 0)
    cols = lax.broadcasted_iota(jnp.int32, (n, n), 1)
    a_ref[...] = g_ref[...]
    w_ref[...] = jnp.where(rows == cols, 1.0, 0.0).astype(w_ref.dtype)
    lane = lax.broadcasted_iota(jnp.int32, (1, n), 1)

    sub = lax.broadcasted_iota(jnp.int32, (8, n), 0)

    def row_of(ref, k, width):
        base = pl.multiple_of((k // 8) * 8, 8)
        block = ref[pl.ds(base, 8), :width]
        return jnp.sum(jnp.where(sub[:, :width] == k - base, block, 0.0), axis=0, keepdims=True)

    def step(k, lo, w_cols):
        row_a = row_of(a_ref, k, n)
        piv = jnp.sum(jnp.where(lane == k, row_a, 0.0))
        col = jnp.broadcast_to(row_a, (8, n)).T[lo:, 0:1]
        ridx = lax.broadcasted_iota(jnp.int32, (n - lo, 1), 0) + lo
        f = jnp.where(ridx > k, col / piv, 0.0)
        a_ref[lo:, lo:] = a_ref[lo:, lo:] - f * row_a[:, lo:]
        w_ref[lo:, :w_cols] = w_ref[lo:, :w_cols] - f * row_of(w_ref, k, w_cols)

    def first(k, c):
        step(k, 0, h)
        return c

    def second(k, c):
        step(k, h, n)
        return c

    lax.fori_loop(0, h, first, 0)
    lax.fori_loop(h, n, second, 0)
    diag = jnp.sum(jnp.where(rows == cols, a_ref[...], 0.0), axis=1, keepdims=True)
    w_ref[...] = w_ref[...] / jnp.sqrt(diag)


def _inverse_cholesky(gram):
    n = gram.shape[0]
    return pl.pallas_call(
        _inverse_cholesky_kernel,
        out_shape=jax.ShapeDtypeStruct((n, n), gram.dtype),
        in_specs=[pl.BlockSpec(memory_space=pltpu.VMEM)],
        out_specs=pl.BlockSpec(memory_space=pltpu.VMEM),
        scratch_shapes=[pltpu.VMEM((n, n), gram.dtype)],
        cost_estimate=pl.CostEstimate(flops=2 * n * n * n, bytes_accessed=8 * n * n, transcendentals=n),
    )(gram)


def shards(panel_cols, affinity):
    local_rows, k = panel_cols.shape
    n_row = lax.axis_size("row")
    n_col = lax.axis_size("col")
    piece = local_rows // n_col
    col_place = lax.axis_index("col")

    gram_part = _dot(panel_cols.T, panel_cols)
    gram_rows = _exchange(gram_part.reshape(n_row, k // n_row, k), "row").sum(0)
    gram_sum = _exchange(jnp.broadcast_to(gram_rows[None], (n_row,) + gram_rows.shape), "row").reshape(k, k)

    own_panel = lax.dynamic_slice_in_dim(panel_cols, col_place * piece, piece, 0)
    panel_stored = _exchange(jnp.broadcast_to(own_panel[None], (n_row, piece, k)), "row").reshape(n_row * piece, k)

    inv_lower = _inverse_cholesky(gram_sum)
    basis_own = _dot(panel_cols, inv_lower.T)
    basis_stored = _dot(panel_stored, inv_lower.T)

    partial_sum = _dot(affinity, basis_stored)
    own_moment = _exchange(partial_sum.reshape(n_col, piece, k), "col").sum(0)
    moment_own = _exchange(jnp.broadcast_to(own_moment[None], (n_col, piece, k)), "col").reshape(local_rows, k)
    band_part = _dot(basis_own.T, moment_own)

    send = jnp.concatenate(
        [
            jnp.broadcast_to(own_moment.reshape(1, piece * k), (n_row, piece * k)),
            band_part.reshape(n_row, (k // n_row) * k),
        ],
        axis=1,
    )
    got = _exchange(send, "row")
    moment_stored = got[:, : piece * k].reshape(n_row * piece, k)
    band_rows = got[:, piece * k :].sum(0)
    band_block = _exchange(jnp.broadcast_to(band_rows[None], (n_row,) + band_rows.shape), "row").reshape(k, k)

    corrected_own = moment_own - 0.5 * _dot(basis_own, band_block)
    corrected_stored = moment_stored - 0.5 * _dot(basis_stored, band_block)
    updated = affinity - _dot(basis_own, corrected_stored.T)
    updated = updated - _dot(corrected_own, basis_stored.T)
    return (updated, band_block)


def solution(mesh):
    placed = (P("row", None), P("row", "col"))
    return jax.shard_map(
        shards, mesh=mesh, in_specs=placed, out_specs=(P("row", "col"), P()), check_vma=False
    )
```

```python
import jax
import jax.numpy as jnp
from jax import lax
from jax.experimental import pallas as pl
from jax.experimental.pallas import tpu as pltpu
from jax.sharding import PartitionSpec as P


def _dot(a, b):
    return jnp.dot(a, b, precision=lax.Precision.HIGHEST)


def _exchange(x, axis):
    return lax.all_to_all(x, axis, 0, 0, tiled=False)


def _inverse_cholesky_kernel(g_ref, w_ref, a_ref):
    n = g_ref.shape[0]
    h = n // 2
    rows = lax.broadcasted_iota(jnp.int32, (n, n), 0)
    cols = lax.broadcasted_iota(jnp.int32, (n, n), 1)
    a_ref[...] = g_ref[...]
    w_ref[...] = jnp.where(rows == cols, 1.0, 0.0).astype(w_ref.dtype)
    lane = lax.broadcasted_iota(jnp.int32, (1, n), 1)

    sub = lax.broadcasted_iota(jnp.int32, (8, n), 0)

    def row_of(ref, k, width):
        base = pl.multiple_of((k // 8) * 8, 8)
        block = ref[pl.ds(base, 8), :width]
        return jnp.sum(jnp.where(sub[:, :width] == k - base, block, 0.0), axis=0, keepdims=True)

    def step(k, lo, w_cols):
        row_a = row_of(a_ref, k, n)
        piv = jnp.sum(jnp.where(lane == k, row_a, 0.0))
        col = jnp.broadcast_to(row_a, (8, n)).T[lo:, 0:1]
        ridx = lax.broadcasted_iota(jnp.int32, (n - lo, 1), 0) + lo
        f = jnp.where(ridx > k, col / piv, 0.0)
        a_ref[lo:, lo:] = a_ref[lo:, lo:] - f * row_a[:, lo:]
        w_ref[lo:, :w_cols] = w_ref[lo:, :w_cols] - f * row_of(w_ref, k, w_cols)

    def first(k, c):
        step(k, 0, h)
        return c

    def second(k, c):
        step(k, h, n)
        return c

    lax.fori_loop(0, h, first, 0, unroll=8)
    lax.fori_loop(h, n, second, 0, unroll=8)
    diag = jnp.sum(jnp.where(rows == cols, a_ref[...], 0.0), axis=1, keepdims=True)
    w_ref[...] = w_ref[...] / jnp.sqrt(diag)


def _inverse_cholesky(gram):
    n = gram.shape[0]
    return pl.pallas_call(
        _inverse_cholesky_kernel,
        out_shape=jax.ShapeDtypeStruct((n, n), gram.dtype),
        in_specs=[pl.BlockSpec(memory_space=pltpu.VMEM)],
        out_specs=pl.BlockSpec(memory_space=pltpu.VMEM),
        scratch_shapes=[pltpu.VMEM((n, n), gram.dtype)],
        cost_estimate=pl.CostEstimate(flops=2 * n * n * n, bytes_accessed=8 * n * n, transcendentals=n),
    )(gram)


def shards(panel_cols, affinity):
    local_rows, k = panel_cols.shape
    n_row = lax.axis_size("row")
    n_col = lax.axis_size("col")
    piece = local_rows // n_col
    col_place = lax.axis_index("col")

    gram_part = _dot(panel_cols.T, panel_cols)
    gram_rows = _exchange(gram_part.reshape(n_row, k // n_row, k), "row").sum(0)
    gram_sum = _exchange(jnp.broadcast_to(gram_rows[None], (n_row,) + gram_rows.shape), "row").reshape(k, k)

    own_panel = lax.dynamic_slice_in_dim(panel_cols, col_place * piece, piece, 0)
    panel_stored = _exchange(jnp.broadcast_to(own_panel[None], (n_row, piece, k)), "row").reshape(n_row * piece, k)

    inv_lower = _inverse_cholesky(gram_sum)
    basis_own = _dot(panel_cols, inv_lower.T)
    basis_stored = _dot(panel_stored, inv_lower.T)

    partial_sum = _dot(affinity, basis_stored)
    own_moment = _exchange(partial_sum.reshape(n_col, piece, k), "col").sum(0)
    moment_own = _exchange(jnp.broadcast_to(own_moment[None], (n_col, piece, k)), "col").reshape(local_rows, k)
    band_part = _dot(basis_own.T, moment_own)

    send = jnp.concatenate(
        [
            jnp.broadcast_to(own_moment.reshape(1, piece * k), (n_row, piece * k)),
            band_part.reshape(n_row, (k // n_row) * k),
        ],
        axis=1,
    )
    got = _exchange(send, "row")
    moment_stored = got[:, : piece * k].reshape(n_row * piece, k)
    band_rows = got[:, piece * k :].sum(0)
    band_block = _exchange(jnp.broadcast_to(band_rows[None], (n_row,) + band_rows.shape), "row").reshape(k, k)

    corrected_own = moment_own - 0.5 * _dot(basis_own, band_block)
    corrected_stored = moment_stored - 0.5 * _dot(basis_stored, band_block)
    updated = affinity - _dot(basis_own, corrected_stored.T)
    updated = updated - _dot(corrected_own, basis_stored.T)
    return (updated, band_block)


def solution(mesh):
    placed = (P("row", None), P("row", "col"))
    return jax.shard_map(
        shards, mesh=mesh, in_specs=placed, out_specs=(P("row", "col"), P()), check_vma=False
    )
```

```python
import jax
import jax.numpy as jnp
from jax import lax
from jax.sharding import PartitionSpec as P


def _dot(a, b):
    return jnp.dot(a, b, precision=lax.Precision.HIGHEST)


def _exchange(x, axis):
    return lax.all_to_all(x, axis, 0, 0, tiled=False)


def _inverse_cholesky(gram):
    h = gram.shape[0] // 2
    eye = jnp.eye(h, dtype=gram.dtype)
    l11 = jnp.linalg.cholesky(gram[:h, :h])
    i11 = jax.scipy.linalg.solve_triangular(l11, eye, lower=True)
    l21 = _dot(gram[h:, :h], i11.T)
    l22 = jnp.linalg.cholesky(gram[h:, h:] - _dot(l21, l21.T))
    i22 = jax.scipy.linalg.solve_triangular(l22, eye, lower=True)
    i21 = -_dot(i22, _dot(l21, i11))
    top = jnp.concatenate([i11, jnp.zeros_like(i11)], axis=1)
    return jnp.concatenate([top, jnp.concatenate([i21, i22], axis=1)], axis=0)


def shards(panel_cols, affinity):
    local_rows, k = panel_cols.shape
    n_row = lax.axis_size("row")
    n_col = lax.axis_size("col")
    piece = local_rows // n_col
    col_place = lax.axis_index("col")

    gram_part = _dot(panel_cols.T, panel_cols)
    gram_rows = _exchange(gram_part.reshape(n_row, k // n_row, k), "row").sum(0)
    gram_sum = _exchange(jnp.broadcast_to(gram_rows[None], (n_row,) + gram_rows.shape), "row").reshape(k, k)

    own_panel = lax.dynamic_slice_in_dim(panel_cols, col_place * piece, piece, 0)
    panel_stored = _exchange(jnp.broadcast_to(own_panel[None], (n_row, piece, k)), "row").reshape(n_row * piece, k)

    inv_lower = _inverse_cholesky(gram_sum)
    basis_own = _dot(panel_cols, inv_lower.T)
    basis_stored = _dot(panel_stored, inv_lower.T)

    partial_sum = _dot(affinity, basis_stored)
    own_moment = _exchange(partial_sum.reshape(n_col, piece, k), "col").sum(0)
    moment_own = _exchange(jnp.broadcast_to(own_moment[None], (n_col, piece, k)), "col").reshape(local_rows, k)
    band_part = _dot(basis_own.T, moment_own)

    send = jnp.concatenate(
        [
            jnp.broadcast_to(own_moment[None], (n_row, piece, k)),
            band_part.reshape(n_row, k // n_row, k),
        ],
        axis=1,
    )
    got = _exchange(send, "row")
    moment_stored = got[:, :piece].reshape(n_row * piece, k)
    band_rows = got[:, piece:].sum(0)
    band_block = _exchange(jnp.broadcast_to(band_rows[None], (n_row,) + band_rows.shape), "row").reshape(k, k)

    corrected_own = moment_own - 0.5 * _dot(basis_own, band_block)
    corrected_stored = moment_stored - 0.5 * _dot(basis_stored, band_block)
    updated = affinity - _dot(basis_own, corrected_stored.T)
    updated = updated - _dot(corrected_own, basis_stored.T)
    return (updated, band_block)


def solution(mesh):
    placed = (P("row", None), P("row", "col"))
    return jax.shard_map(
        shards, mesh=mesh, in_specs=placed, out_specs=(P("row", "col"), P()), check_vma=False
    )
```

```python
import jax
import jax.numpy as jnp
from jax import lax
from jax.experimental import pallas as pl
from jax.experimental.pallas import tpu as pltpu
from jax.sharding import PartitionSpec as P


def _dot(a, b):
    return jnp.dot(a, b, precision=lax.Precision.HIGHEST)


def _exchange(x, axis):
    return lax.all_to_all(x, axis, 0, 0, tiled=False)


def _inverse_cholesky_kernel(g_ref, w_ref, a_ref):
    n = g_ref.shape[0]
    rows = lax.broadcasted_iota(jnp.int32, (n, n), 0)
    cols = lax.broadcasted_iota(jnp.int32, (n, n), 1)
    a_ref[...] = g_ref[...]
    w_ref[...] = jnp.where(rows == cols, 1.0, 0.0).astype(w_ref.dtype)
    lane = lax.broadcasted_iota(jnp.int32, (8, n), 1)
    sub = lax.broadcasted_iota(jnp.int32, (8, 1), 0)

    def block(b, carry):
        k0 = pl.multiple_of(b * 8, 8)
        r = a_ref[pl.ds(k0, 8), :]
        wb = w_ref[pl.ds(k0, 8), :]
        scale = jnp.zeros((8, 1), r.dtype)
        for s in range(8):
            k = k0 + s
            row = r[s : s + 1, :]
            piv = jnp.sum(jnp.where(lane[0:1] == k, row, 0.0))
            col = jnp.sum(jnp.where(lane == k, r, 0.0), axis=1, keepdims=True)
            fb = jnp.where(sub > s, col / piv, 0.0)
            r = r - fb * row
            wb = wb - fb * wb[s : s + 1, :]
            scale = jnp.where(sub == s, 1.0 / piv, scale)
        f = jnp.where(lane >= k0 + 8, r * scale, 0.0).T
        a_ref[pl.ds(k0, 8), :] = r
        w_ref[pl.ds(k0, 8), :] = wb
        for c0 in range(0, n, 32):
            fc = f[c0 : c0 + 32, :]
            upd_a = a_ref[c0 : c0 + 32, :]
            upd_w = w_ref[c0 : c0 + 32, :]
            for s in range(8):
                upd_a = upd_a - fc[:, s : s + 1] * r[s : s + 1, :]
                upd_w = upd_w - fc[:, s : s + 1] * wb[s : s + 1, :]
            a_ref[c0 : c0 + 32, :] = upd_a
            w_ref[c0 : c0 + 32, :] = upd_w
        return carry

    lax.fori_loop(0, n // 8, block, 0)
    diag = jnp.sum(jnp.where(rows == cols, a_ref[...], 0.0), axis=1, keepdims=True)
    w_ref[...] = w_ref[...] / jnp.sqrt(diag)


def _inverse_cholesky(gram):
    n = gram.shape[0]
    return pl.pallas_call(
        _inverse_cholesky_kernel,
        out_shape=jax.ShapeDtypeStruct((n, n), gram.dtype),
        in_specs=[pl.BlockSpec(memory_space=pltpu.VMEM)],
        out_specs=pl.BlockSpec(memory_space=pltpu.VMEM),
        scratch_shapes=[pltpu.VMEM((n, n), gram.dtype)],
        cost_estimate=pl.CostEstimate(flops=2 * n * n * n, bytes_accessed=8 * n * n, transcendentals=n),
    )(gram)


def shards(panel_cols, affinity):
    local_rows, k = panel_cols.shape
    n_row = lax.axis_size("row")
    n_col = lax.axis_size("col")
    piece = local_rows // n_col
    col_place = lax.axis_index("col")

    gram_part = _dot(panel_cols.T, panel_cols)
    gram_rows = _exchange(gram_part.reshape(n_row, k // n_row, k), "row").sum(0)
    gram_sum = _exchange(jnp.broadcast_to(gram_rows[None], (n_row,) + gram_rows.shape), "row").reshape(k, k)

    own_panel = lax.dynamic_slice_in_dim(panel_cols, col_place * piece, piece, 0)
    panel_stored = _exchange(jnp.broadcast_to(own_panel[None], (n_row, piece, k)), "row").reshape(n_row * piece, k)

    inv_lower = _inverse_cholesky(gram_sum)
    basis_own = _dot(panel_cols, inv_lower.T)
    basis_stored = _dot(panel_stored, inv_lower.T)

    partial_sum = _dot(affinity, basis_stored)
    own_moment = _exchange(partial_sum.reshape(n_col, piece, k), "col").sum(0)
    moment_own = _exchange(jnp.broadcast_to(own_moment[None], (n_col, piece, k)), "col").reshape(local_rows, k)
    band_part = _dot(basis_own.T, moment_own)

    send = jnp.concatenate(
        [
            jnp.broadcast_to(own_moment.reshape(1, piece * k), (n_row, piece * k)),
            band_part.reshape(n_row, (k // n_row) * k),
        ],
        axis=1,
    )
    got = _exchange(send, "row")
    moment_stored = got[:, : piece * k].reshape(n_row * piece, k)
    band_rows = got[:, piece * k :].sum(0)
    band_block = _exchange(jnp.broadcast_to(band_rows[None], (n_row,) + band_rows.shape), "row").reshape(k, k)

    corrected_own = moment_own - 0.5 * _dot(basis_own, band_block)
    corrected_stored = moment_stored - 0.5 * _dot(basis_stored, band_block)
    updated = affinity - _dot(basis_own, corrected_stored.T)
    updated = updated - _dot(corrected_own, basis_stored.T)
    return (updated, band_block)


def solution(mesh):
    placed = (P("row", None), P("row", "col"))
    return jax.shard_map(
        shards, mesh=mesh, in_specs=placed, out_specs=(P("row", "col"), P()), check_vma=False
    )
```

```python
import jax
import jax.numpy as jnp
from jax import lax
from jax.experimental import pallas as pl
from jax.experimental.pallas import tpu as pltpu
from jax.sharding import PartitionSpec as P


def _dot(a, b):
    return jnp.dot(a, b, precision=lax.Precision.HIGHEST)


def _exchange(x, axis):
    return lax.all_to_all(x, axis, 0, 0, tiled=False)


def _inverse_cholesky_kernel(g_ref, w_ref, a_ref):
    n = g_ref.shape[0]
    rows = lax.broadcasted_iota(jnp.int32, (n, n), 0)
    cols = lax.broadcasted_iota(jnp.int32, (n, n), 1)
    a_ref[...] = g_ref[...]
    w_ref[...] = jnp.where(rows == cols, 1.0, 0.0).astype(w_ref.dtype)
    sub = lax.broadcasted_iota(jnp.int32, (8, 1), 0)

    def block(b, lo, wc):
        k0 = pl.multiple_of(b * 8, 8)
        lane = lax.broadcasted_iota(jnp.int32, (8, n - lo), 1) + lo
        r = a_ref[pl.ds(k0, 8), lo:]
        wb = w_ref[pl.ds(k0, 8), :wc]
        scale = jnp.zeros((8, 1), r.dtype)
        for s in range(8):
            k = k0 + s
            row = r[s : s + 1, :]
            col = jnp.sum(jnp.where(lane == k, r, 0.0), axis=1, keepdims=True)
            piv = col[s : s + 1, :]
            fb = jnp.where(sub > s, col / piv, 0.0)
            r = r - fb * row
            wb = wb - fb * wb[s : s + 1, :]
            scale = jnp.where(sub == s, 1.0 / piv, scale)
        f = jnp.where(lane >= k0 + 8, r * scale, 0.0).T
        a_ref[pl.ds(k0, 8), lo:] = r
        w_ref[pl.ds(k0, 8), :wc] = wb
        for c0 in range(lo, n, 32):

            @pl.when(c0 + 32 > k0 + 8)
            def _():
                fc = f[c0 - lo : c0 - lo + 32, :]
                upd_a = a_ref[c0 : c0 + 32, lo:]
                upd_w = w_ref[c0 : c0 + 32, :wc]
                for s in range(8):
                    upd_a = upd_a - fc[:, s : s + 1] * r[s : s + 1, :]
                    upd_w = upd_w - fc[:, s : s + 1] * wb[s : s + 1, :]
                a_ref[c0 : c0 + 32, lo:] = upd_a
                w_ref[c0 : c0 + 32, :wc] = upd_w

    h = n // 2

    def first(b, carry):
        block(b, 0, h)
        return carry

    def second(b, carry):
        block(b, h, n)
        return carry

    lax.fori_loop(0, h // 8, first, 0)
    lax.fori_loop(h // 8, n // 8, second, 0)
    diag = jnp.sum(jnp.where(rows == cols, a_ref[...], 0.0), axis=1, keepdims=True)
    w_ref[...] = w_ref[...] / jnp.sqrt(diag)


def _inverse_cholesky(gram):
    n = gram.shape[0]
    return pl.pallas_call(
        _inverse_cholesky_kernel,
        out_shape=jax.ShapeDtypeStruct((n, n), gram.dtype),
        in_specs=[pl.BlockSpec(memory_space=pltpu.VMEM)],
        out_specs=pl.BlockSpec(memory_space=pltpu.VMEM),
        scratch_shapes=[pltpu.VMEM((n, n), gram.dtype)],
        cost_estimate=pl.CostEstimate(flops=2 * n * n * n, bytes_accessed=8 * n * n, transcendentals=n),
    )(gram)


def shards(panel_cols, affinity):
    local_rows, k = panel_cols.shape
    n_row = lax.axis_size("row")
    n_col = lax.axis_size("col")
    piece = local_rows // n_col
    col_place = lax.axis_index("col")

    gram_part = _dot(panel_cols.T, panel_cols)
    gram_rows = _exchange(gram_part.reshape(n_row, k // n_row, k), "row").sum(0)
    gram_sum = _exchange(jnp.broadcast_to(gram_rows[None], (n_row,) + gram_rows.shape), "row").reshape(k, k)

    own_panel = lax.dynamic_slice_in_dim(panel_cols, col_place * piece, piece, 0)
    panel_stored = _exchange(jnp.broadcast_to(own_panel[None], (n_row, piece, k)), "row").reshape(n_row * piece, k)

    inv_lower = _inverse_cholesky(gram_sum)
    basis_own = _dot(panel_cols, inv_lower.T)
    basis_stored = _dot(panel_stored, inv_lower.T)

    partial_sum = _dot(affinity, basis_stored)
    own_moment = _exchange(partial_sum.reshape(n_col, piece, k), "col").sum(0)
    moment_own = _exchange(jnp.broadcast_to(own_moment[None], (n_col, piece, k)), "col").reshape(local_rows, k)
    band_part = _dot(basis_own.T, moment_own)

    send = jnp.concatenate(
        [
            jnp.broadcast_to(own_moment.reshape(1, piece * k), (n_row, piece * k)),
            band_part.reshape(n_row, (k // n_row) * k),
        ],
        axis=1,
    )
    got = _exchange(send, "row")
    moment_stored = got[:, : piece * k].reshape(n_row * piece, k)
    band_rows = got[:, piece * k :].sum(0)
    band_block = _exchange(jnp.broadcast_to(band_rows[None], (n_row,) + band_rows.shape), "row").reshape(k, k)

    corrected_own = moment_own - 0.5 * _dot(basis_own, band_block)
    corrected_stored = moment_stored - 0.5 * _dot(basis_stored, band_block)
    updated = affinity - _dot(basis_own, corrected_stored.T)
    updated = updated - _dot(corrected_own, basis_stored.T)
    return (updated, band_block)


def solution(mesh):
    placed = (P("row", None), P("row", "col"))
    return jax.shard_map(
        shards, mesh=mesh, in_specs=placed, out_specs=(P("row", "col"), P()), check_vma=False
    )
```

```python
import jax
import jax.numpy as jnp
from jax import lax
from jax.experimental import pallas as pl
from jax.experimental.pallas import tpu as pltpu
from jax.sharding import PartitionSpec as P


def _dot(a, b):
    return jnp.dot(a, b, precision=lax.Precision.HIGHEST)


def _exchange(x, axis):
    return lax.all_to_all(x, axis, 0, 0, tiled=False)


def _inverse_cholesky_kernel(g_ref, w_ref, a_ref):
    n = g_ref.shape[0]
    rows = lax.broadcasted_iota(jnp.int32, (n, n), 0)
    cols = lax.broadcasted_iota(jnp.int32, (n, n), 1)
    a_ref[...] = g_ref[...]
    w_ref[...] = jnp.where(rows == cols, 1.0, 0.0).astype(w_ref.dtype)
    sub = lax.broadcasted_iota(jnp.int32, (8, 1), 0)

    def block(b, lo, wc):
        k0 = pl.multiple_of(b * 8, 8)
        lane = lax.broadcasted_iota(jnp.int32, (8, n - lo), 1) + lo
        r = a_ref[pl.ds(k0, 8), lo:]
        wb = w_ref[pl.ds(k0, 8), :wc]
        scale = jnp.zeros((8, 1), r.dtype)
        for s in range(8):
            k = k0 + s
            row = r[s : s + 1, :]
            col = jnp.sum(jnp.where(lane == k, r, 0.0), axis=1, keepdims=True)
            piv = col[s : s + 1, :]
            fb = jnp.where(sub > s, col / piv, 0.0)
            r = r - fb * row
            wb = wb - fb * wb[s : s + 1, :]
            scale = jnp.where(sub == s, 1.0 / piv, scale)
        f = jnp.where(lane >= k0 + 8, r * scale, 0.0).T
        a_ref[pl.ds(k0, 8), lo:] = r
        w_ref[pl.ds(k0, 8), :wc] = wb
        for c0 in range(lo, n, 32):

            @pl.when(c0 + 32 > k0 + 8)
            def _():
                fc = f[c0 - lo : c0 - lo + 32, :]
                upd_a = a_ref[c0 : c0 + 32, lo:]
                upd_w = w_ref[c0 : c0 + 32, :wc]
                for s in range(8):
                    upd_a = upd_a - fc[:, s : s + 1] * r[s : s + 1, :]
                    upd_w = upd_w - fc[:, s : s + 1] * wb[s : s + 1, :]
                a_ref[c0 : c0 + 32, lo:] = upd_a
                w_ref[c0 : c0 + 32, :wc] = upd_w

    h = n // 2

    def first(b, carry):
        block(b, 0, h)
        return carry

    def second(b, carry):
        block(b, h, n)
        return carry

    lax.fori_loop(0, h // 8, first, 0)
    lax.fori_loop(h // 8, n // 8, second, 0)
    diag = jnp.sum(jnp.where(rows == cols, a_ref[...], 0.0), axis=1, keepdims=True)
    w_ref[...] = w_ref[...] / jnp.sqrt(diag)


def _inverse_cholesky(gram):
    n = gram.shape[0]
    return pl.pallas_call(
        _inverse_cholesky_kernel,
        out_shape=jax.ShapeDtypeStruct((n, n), gram.dtype),
        in_specs=[pl.BlockSpec(memory_space=pltpu.VMEM)],
        out_specs=pl.BlockSpec(memory_space=pltpu.VMEM),
        scratch_shapes=[pltpu.VMEM((n, n), gram.dtype)],
        cost_estimate=pl.CostEstimate(flops=2 * n * n * n, bytes_accessed=8 * n * n, transcendentals=n),
    )(gram)


def shards(panel_cols, affinity):
    local_rows, k = panel_cols.shape
    n_row = lax.axis_size("row")
    n_col = lax.axis_size("col")
    piece = local_rows // n_col
    col_place = lax.axis_index("col")

    gram_part = _dot(panel_cols.T, panel_cols)
    gram_rows = _exchange(gram_part.reshape(n_row, k // n_row, k), "row").sum(0)
    gram_sum = _exchange(jnp.broadcast_to(gram_rows[None], (n_row,) + gram_rows.shape), "row").reshape(k, k)

    own_panel = lax.dynamic_slice_in_dim(panel_cols, col_place * piece, piece, 0)
    panel_stored = _exchange(jnp.broadcast_to(own_panel[None], (n_row, piece, k)), "row").reshape(n_row * piece, k)

    inv_lower = _inverse_cholesky(gram_sum)
    basis_own = _dot(panel_cols, inv_lower.T)
    basis_stored = _dot(panel_stored, inv_lower.T)

    partial_sum = _dot(affinity, basis_stored)
    own_moment = _exchange(partial_sum.reshape(n_col, piece, k), "col").sum(0)
    moment_own = _exchange(jnp.broadcast_to(own_moment[None], (n_col, piece, k)), "col").reshape(local_rows, k)
    band_part = _dot(basis_own.T, moment_own)

    send = jnp.concatenate(
        [
            jnp.broadcast_to(own_moment.reshape(1, piece * k), (n_row, piece * k)),
            band_part.reshape(n_row, (k // n_row) * k),
        ],
        axis=1,
    )
    got = _exchange(send, "row")
    moment_stored = got[:, : piece * k].reshape(n_row * piece, k)
    band_rows = got[:, piece * k :].sum(0)
    band_block = _exchange(jnp.broadcast_to(band_rows[None], (n_row,) + band_rows.shape), "row").reshape(k, k)

    left = jnp.concatenate([basis_own, moment_own], axis=1)
    right = jnp.concatenate([moment_stored, basis_stored], axis=1)
    updated = affinity - _dot(left, right.T)
    sym_band = 0.5 * (band_block + band_block.T)
    updated = updated + _dot(_dot(basis_own, sym_band), basis_stored.T)
    return (updated, band_block)


def solution(mesh):
    placed = (P("row", None), P("row", "col"))
    return jax.shard_map(
        shards, mesh=mesh, in_specs=placed, out_specs=(P("row", "col"), P()), check_vma=False
    )
```

```python
import jax
import jax.numpy as jnp
from jax import lax
from jax.experimental import pallas as pl
from jax.experimental.pallas import tpu as pltpu
from jax.sharding import PartitionSpec as P


def _dot(a, b):
    return jnp.dot(a, b, precision=lax.Precision.HIGHEST)


def _exchange(x, axis):
    return lax.all_to_all(x, axis, 0, 0, tiled=False)


def _inverse_cholesky_kernel(g_ref, w_ref, a_ref):
    n = g_ref.shape[0]
    rows = lax.broadcasted_iota(jnp.int32, (n, n), 0)
    cols = lax.broadcasted_iota(jnp.int32, (n, n), 1)
    a_ref[...] = g_ref[...]
    w_ref[...] = jnp.where(rows == cols, 1.0, 0.0).astype(w_ref.dtype)
    sub = lax.broadcasted_iota(jnp.int32, (8, 1), 0)

    def block(b, lo, wc):
        k0 = pl.multiple_of(b * 8, 8)
        lane = lax.broadcasted_iota(jnp.int32, (8, n - lo), 1) + lo
        r = a_ref[pl.ds(k0, 8), lo:]
        wb = w_ref[pl.ds(k0, 8), :wc]
        scale = jnp.zeros((8, 1), r.dtype)
        for s in range(8):
            k = k0 + s
            row = r[s : s + 1, :]
            col = jnp.sum(jnp.where(lane == k, r, 0.0), axis=1, keepdims=True)
            piv = col[s : s + 1, :]
            fb = jnp.where(sub > s, col / piv, 0.0)
            r = r - fb * row
            wb = wb - fb * wb[s : s + 1, :]
            scale = jnp.where(sub == s, 1.0 / piv, scale)
        f = jnp.where(lane >= k0 + 8, r * scale, 0.0).T
        a_ref[pl.ds(k0, 8), lo:] = r
        w_ref[pl.ds(k0, 8), :wc] = wb
        for c0 in range(lo, n, 32):

            @pl.when(c0 + 32 > k0 + 8)
            def _():
                fc = f[c0 - lo : c0 - lo + 32, :]
                upd_a = a_ref[c0 : c0 + 32, lo:]
                upd_w = w_ref[c0 : c0 + 32, :wc]
                for s in range(8):
                    upd_a = upd_a - fc[:, s : s + 1] * r[s : s + 1, :]
                    upd_w = upd_w - fc[:, s : s + 1] * wb[s : s + 1, :]
                a_ref[c0 : c0 + 32, lo:] = upd_a
                w_ref[c0 : c0 + 32, :wc] = upd_w

    h = n // 2

    def first(b, carry):
        block(b, 0, h)
        return carry

    def second(b, carry):
        block(b, h, n)
        return carry

    lax.fori_loop(0, h // 8, first, 0)
    lax.fori_loop(h // 8, n // 8, second, 0)
    diag = jnp.sum(jnp.where(rows == cols, a_ref[...], 0.0), axis=1, keepdims=True)
    w_ref[...] = w_ref[...] / jnp.sqrt(diag)


def _inverse_cholesky(gram):
    n = gram.shape[0]
    return pl.pallas_call(
        _inverse_cholesky_kernel,
        out_shape=jax.ShapeDtypeStruct((n, n), gram.dtype),
        in_specs=[pl.BlockSpec(memory_space=pltpu.VMEM)],
        out_specs=pl.BlockSpec(memory_space=pltpu.VMEM),
        scratch_shapes=[pltpu.VMEM((n, n), gram.dtype)],
        cost_estimate=pl.CostEstimate(flops=2 * n * n * n, bytes_accessed=8 * n * n, transcendentals=n),
    )(gram)


def shards(panel_cols, affinity):
    local_rows, k = panel_cols.shape
    n_row = lax.axis_size("row")
    n_col = lax.axis_size("col")
    piece = local_rows // n_col
    col_place = lax.axis_index("col")

    gram_part = _dot(panel_cols.T, panel_cols)
    gram_rows = _exchange(gram_part.reshape(n_row, k // n_row, k), "row").sum(0)
    gram_sum = _exchange(jnp.broadcast_to(gram_rows[None], (n_row,) + gram_rows.shape), "row").reshape(k, k)

    own_panel = lax.dynamic_slice_in_dim(panel_cols, col_place * piece, piece, 0)
    panel_stored = _exchange(jnp.broadcast_to(own_panel[None], (n_row, piece, k)), "row").reshape(n_row * piece, k)

    inv_lower = _inverse_cholesky(gram_sum)
    basis_own = _dot(panel_cols, inv_lower.T)
    basis_stored = _dot(panel_stored, inv_lower.T)

    partial_sum = _dot(affinity, basis_stored)
    own_moment = _exchange(partial_sum.reshape(n_col, piece, k), "col").sum(0)
    moment_own = _exchange(jnp.broadcast_to(own_moment[None], (n_col, piece, k)), "col").reshape(local_rows, k)
    band_part = _dot(basis_own.T, moment_own)

    lanes = 128
    m_rows = piece * k // lanes
    send = jnp.concatenate(
        [
            jnp.broadcast_to(own_moment.reshape(1, m_rows, lanes), (n_row, m_rows, lanes)),
            band_part.reshape(n_row, (k // n_row) * k // lanes, lanes),
        ],
        axis=1,
    )
    got = _exchange(send, "row")
    moment_stored = got[:, :m_rows].reshape(n_row * piece, k)
    band_rows = got[:, m_rows:].sum(0).reshape(k // n_row, k)
    band_block = _exchange(jnp.broadcast_to(band_rows[None], (n_row,) + band_rows.shape), "row").reshape(k, k)

    left = jnp.concatenate([basis_own, moment_own], axis=1)
    right = jnp.concatenate([moment_stored, basis_stored], axis=1)
    updated = affinity - _dot(left, right.T)
    sym_band = 0.5 * (band_block + band_block.T)
    updated = updated + _dot(_dot(basis_own, sym_band), basis_stored.T)
    return (updated, band_block)


def solution(mesh):
    placed = (P("row", None), P("row", "col"))
    return jax.shard_map(
        shards, mesh=mesh, in_specs=placed, out_specs=(P("row", "col"), P()), check_vma=False
    )
```

```python
import jax
import jax.numpy as jnp
from jax import lax
from jax.experimental import pallas as pl
from jax.experimental.pallas import tpu as pltpu
from jax.sharding import PartitionSpec as P


def _dot(a, b):
    return jnp.dot(a, b, precision=lax.Precision.HIGHEST)


def _exchange(x, axis):
    return lax.all_to_all(x, axis, 0, 0, tiled=False)


def _inverse_cholesky_kernel(g_ref, w_ref, a_ref):
    n = g_ref.shape[0]
    rows = lax.broadcasted_iota(jnp.int32, (n, n), 0)
    cols = lax.broadcasted_iota(jnp.int32, (n, n), 1)
    a_ref[...] = g_ref[...]
    w_ref[...] = jnp.where(rows == cols, 1.0, 0.0).astype(w_ref.dtype)
    sub = lax.broadcasted_iota(jnp.int32, (8, 1), 0)

    def block(b, lo, wc):
        k0 = pl.multiple_of(b * 8, 8)
        lane = lax.broadcasted_iota(jnp.int32, (8, n - lo), 1) + lo
        r = a_ref[pl.ds(k0, 8), lo:]
        wb = w_ref[pl.ds(k0, 8), :wc]
        scale = jnp.zeros((8, 1), r.dtype)
        for s in range(8):
            k = k0 + s
            row = r[s : s + 1, :]
            col = jnp.sum(jnp.where(lane == k, r, 0.0), axis=1, keepdims=True)
            piv = col[s : s + 1, :]
            fb = jnp.where(sub > s, col / piv, 0.0)
            r = r - fb * row
            wb = wb - fb * wb[s : s + 1, :]
            scale = jnp.where(sub == s, 1.0 / piv, scale)
        f = jnp.where(lane >= k0 + 8, r * scale, 0.0).T
        a_ref[pl.ds(k0, 8), lo:] = r
        w_ref[pl.ds(k0, 8), :wc] = wb
        for c0 in range(lo, n, 32):

            @pl.when(c0 + 32 > k0 + 8)
            def _():
                fc = f[c0 - lo : c0 - lo + 32, :]
                upd_a = a_ref[c0 : c0 + 32, lo:]
                upd_w = w_ref[c0 : c0 + 32, :wc]
                for s in range(8):
                    upd_a = upd_a - fc[:, s : s + 1] * r[s : s + 1, :]
                    upd_w = upd_w - fc[:, s : s + 1] * wb[s : s + 1, :]
                a_ref[c0 : c0 + 32, lo:] = upd_a
                w_ref[c0 : c0 + 32, :wc] = upd_w

    h = n // 2

    def first(b, carry):
        block(b, 0, h)
        return carry

    def second(b, carry):
        block(b, h, n)
        return carry

    lax.fori_loop(0, h // 8, first, 0)
    lax.fori_loop(h // 8, n // 8, second, 0)
    diag = jnp.sum(jnp.where(rows == cols, a_ref[...], 0.0), axis=1, keepdims=True)
    w_ref[...] = w_ref[...] / jnp.sqrt(diag)


def _inverse_cholesky(gram):
    n = gram.shape[0]
    return pl.pallas_call(
        _inverse_cholesky_kernel,
        out_shape=jax.ShapeDtypeStruct((n, n), gram.dtype),
        in_specs=[pl.BlockSpec(memory_space=pltpu.VMEM)],
        out_specs=pl.BlockSpec(memory_space=pltpu.VMEM),
        scratch_shapes=[pltpu.VMEM((n, n), gram.dtype)],
        cost_estimate=pl.CostEstimate(flops=2 * n * n * n, bytes_accessed=8 * n * n, transcendentals=n),
    )(gram)


def shards(panel_cols, affinity):
    local_rows, k = panel_cols.shape
    n_row = lax.axis_size("row")
    n_col = lax.axis_size("col")
    piece = local_rows // n_col
    col_place = lax.axis_index("col")

    gram_part = _dot(panel_cols.T, panel_cols)
    gram_rows = _exchange(gram_part.reshape(n_row, k // n_row, k), "row").sum(0)
    gram_sum = _exchange(jnp.broadcast_to(gram_rows[None], (n_row,) + gram_rows.shape), "row").reshape(k, k)

    own_panel = lax.dynamic_slice_in_dim(panel_cols, col_place * piece, piece, 0)
    panel_stored = _exchange(jnp.broadcast_to(own_panel[None], (n_row, piece, k)), "row").reshape(n_row * piece, k)

    inv_lower = _inverse_cholesky(gram_sum)
    basis_own = _dot(panel_cols, inv_lower.T)
    basis_stored = _dot(panel_stored, inv_lower.T)

    partial_sum = _dot(affinity, basis_stored)
    own_moment = _exchange(partial_sum.reshape(n_col, piece, k), "col").sum(0)
    moment_own = _exchange(jnp.broadcast_to(own_moment[None], (n_col, piece, k)), "col").reshape(local_rows, k)
    band_part = _dot(basis_own.T, moment_own)

    lanes = min(128, k)
    parts = k // lanes
    m_block = own_moment.reshape(piece, parts, lanes).transpose(1, 0, 2).reshape(parts * piece, lanes)
    send = jnp.concatenate(
        [
            jnp.broadcast_to(m_block[None], (n_row, parts * piece, lanes)),
            band_part.reshape(n_row, -1, lanes),
        ],
        axis=1,
    )
    got = _exchange(send, "row")
    moment_parts = [got[:, h * piece : (h + 1) * piece].reshape(n_row * piece, lanes) for h in range(parts)]
    band_rows = got[:, parts * piece :].sum(0).reshape(k // n_row, k)
    band_block = _exchange(jnp.broadcast_to(band_rows[None], (n_row,) + band_rows.shape), "row").reshape(k, k)

    updated = affinity - _dot(moment_own, basis_stored.T)
    for h, part in enumerate(moment_parts):
        updated = updated - _dot(basis_own[:, h * lanes : (h + 1) * lanes], part.T)
    sym_band = 0.5 * (band_block + band_block.T)
    updated = updated + _dot(_dot(basis_own, sym_band), basis_stored.T)
    return (updated, band_block)


def solution(mesh):
    placed = (P("row", None), P("row", "col"))
    return jax.shard_map(
        shards, mesh=mesh, in_specs=placed, out_specs=(P("row", "col"), P()), check_vma=False
    )
```
